1024 devices in a mesh: section: 8 (over x), dp: 128 (over z, y, core).
Axes of the slice: x: 8, y: 8, z: 8, core: 2. Of those that a mesh axis runs over, the one named last changes fastest.
Arguments:
- images: bfloat16 [4, 128, 10, 10, 352], P(None, 'dp'), may hold values from -6 to 6
- cotangent: bfloat16 [4, 128, 10, 10, 352], P(None, 'dp'), may hold values from -6 to 6
- dw_kernel: float32 [8, 49, 352], P('section'), may hold values from -0.875 to 0.875
- layer_scale: float32 [8, 352], P('section'), may hold values from 0.2 to 2
- w_in: bfloat16 [8, 1408, 352], P('section'), may hold values from -0.3125 to 0.3125
- w_out: bfloat16 [8, 1408, 352], P('section'), may hold values from -0.15625 to 0.15625
Outputs:
- grad_in: float32 [8, 1408, 352], P('section', 'dp')
- input_grads: bfloat16 [8, 4, 128, 10, 10, 352], P('section', None, 'dp')
The draws below stay inside these ranges and needn't reach their ends.
All inputs are finite; a program needn't handle non-finite values.
Results may differ from the reference program's by a relative error of at most 0.024.
Values may be sent and summed in bfloat16 or wider, within the bound.
No kernel may reach another device: no remote copies, remote signals or barrier semaphores. Data moves between devices by JAX's collectives and lax.ppermute only.
A program may use at most 32 MiB of HBM per device.

```python
import math
import jax
import jax.numpy as jnp
from jax import lax

C = 352
HID = 1408
KS = 7
SIDE = 10
MB = 4
IMG = 1
SECTIONS = 8
BATCH = 128


def level_of(stream_key, dims, shards, least, top_value):
    loudness = 1.0
    for dim, blocks in shards:
        steps = jax.random.uniform(jax.random.fold_in(jax.random.fold_in(stream_key, 6), dim), (blocks,), jnp.float32, least / len(shards), top_value / len(shards))
        loudness = loudness * jnp.repeat(jnp.exp(steps), dims[dim] // blocks).reshape((-1,) + (1,) * (len(dims) - 1 - dim))
    return loudness


def noise(stream_key, extent, deviation, limit, cuts=(), dtype=jnp.bfloat16):
    factor_of = level_of(stream_key, extent, cuts, -0.22, 0.18) if cuts else 1.0
    drawn = jax.random.normal(stream_key, extent, jnp.float32) * deviation * factor_of
    return jnp.minimum(jnp.maximum(drawn, -limit), limit).astype(dtype)


def setup_inputs(seed: int = 0) -> dict:
    key_list = jax.random.split(jax.random.key(seed), 7)
    images = noise(key_list[0], (MB, BATCH, SIDE, SIDE, C), 1.0, 6.0, ((1, 128),))
    cotangent = noise(key_list[1], (MB, BATCH, SIDE, SIDE, C), 1.0, 6.0, ((1, 128),))
    dw_kernel = noise(key_list[2], (SECTIONS, KS * KS, C), (KS * KS) ** -0.5, 0.875, ((0, 8),), jnp.float32)
    layer_scale = jnp.clip(jnp.exp(math.log(2.0) - 2.3025851 * jax.random.uniform(key_list[3], (SECTIONS, C), jnp.float32) ** level_of(key_list[3], (SECTIONS, C), ((0, 8),), -0.2, 0.2)), 0.2, 2.0)
    w_in = noise(key_list[4], (SECTIONS, HID, C), C ** -0.5, 0.3125, ((0, 8),))
    w_out = noise(key_list[5], (SECTIONS, HID, C), HID ** -0.5, 0.15625, ((0, 8),))
    return dict(images=images, cotangent=cotangent, dw_kernel=dw_kernel, layer_scale=layer_scale, w_in=w_in, w_out=w_out)


EPS = 1e-06

def depthwise(field, kernel):
    reach = KS // 2
    height = field.shape[1]
    padded = jnp.pad(field, ((0, 0), (reach, reach), (reach, reach), (0, 0)))
    total = jnp.zeros(field.shape, jnp.float32)
    for row in range(KS):
        for col in range(KS):
            total = total + padded[:, row:row + height, col:col + height, :] * kernel[row * KS + col]
    return total

def depthwise_adjoint(field, kernel):
    reach = KS // 2
    height = field.shape[1]
    padded = jnp.pad(field, ((0, 0), (reach, reach), (reach, reach), (0, 0)))
    total = jnp.zeros(field.shape, jnp.float32)
    for row in range(KS):
        for col in range(KS):
            top = 2 * reach - row
            left = 2 * reach - col
            total = total + padded[:, top:top + height, left:left + height, :] * kernel[row * KS + col]
    return total

def gelu_parts(value):
    normal_cdf = 0.5 * (1.0 + lax.erf(value * 0.7071067811865476))
    density = jnp.exp(-0.5 * value * value) * 0.3989422804014327
    return (value * normal_cdf, normal_cdf + value * density)

def block_inner(inputs, kernel, weight_in):
    width = inputs.shape[-1]
    mixed = depthwise(inputs.astype(jnp.float32), kernel)
    center = mixed - lax.optimization_barrier(jnp.mean(mixed, axis=-1, keepdims=True))
    inv_std = lax.rsqrt(lax.optimization_barrier(jnp.mean(center * center, axis=-1, keepdims=True)) + EPS)
    normed = center * inv_std
    flat = normed.reshape(-1, width).astype(jnp.bfloat16)
    pre = lax.dot_general(flat, weight_in, (((1,), (1,)), ((), ())), preferred_element_type=jnp.float32)
    active, slope = gelu_parts(pre)
    hidden = active.astype(jnp.bfloat16)
    return (normed, inv_std, flat, slope, hidden)

def block_forward(inputs, kernel, scale, weight_in, weight_out):
    width = inputs.shape[-1]
    normed, inv_std, flat, slope, hidden = block_inner(inputs, kernel, weight_in)
    branch = jnp.dot(hidden, weight_out, preferred_element_type=jnp.float32)
    output = inputs.reshape(-1, width).astype(jnp.float32) + scale * branch
    return output.astype(jnp.bfloat16).reshape(inputs.shape)

def block_backward(inputs, upstream, kernel, scale, weight_in, weight_out):
    width = inputs.shape[-1]
    normed, inv_std, flat, slope, hidden = block_inner(inputs, kernel, weight_in)
    up_flat = upstream.reshape(-1, width).astype(jnp.float32)
    branch_grad = (scale * up_flat).astype(jnp.bfloat16)
    hidden_grad = lax.dot_general(branch_grad, weight_out, (((1,), (1,)), ((), ())), preferred_element_type=jnp.float32)
    pre_grad = (hidden_grad * slope).astype(jnp.bfloat16)
    normed_grad = jnp.dot(pre_grad, weight_in, preferred_element_type=jnp.float32).reshape(inputs.shape)
    mean_grad = lax.optimization_barrier(jnp.mean(normed_grad, axis=-1, keepdims=True))
    mean_cross = lax.optimization_barrier(jnp.mean(normed_grad * normed, axis=-1, keepdims=True))
    mixed_grad = inv_std * (normed_grad - mean_grad - normed * mean_cross)
    input_grad = (upstream.astype(jnp.float32) + depthwise_adjoint(mixed_grad, kernel)).astype(jnp.bfloat16)
    return (input_grad, flat, pre_grad)

def reference(images, cotangent, dw_kernel, layer_scale, w_in, w_out):
    micro_count, batch_size, side, _, width = images.shape
    field = images.reshape(micro_count * batch_size, side, side, width)
    kept = []
    for section in range(SECTIONS):
        kept.append(field)
        field = block_forward(field, dw_kernel[section], layer_scale[section], w_in[section], w_out[section])
    upstream = cotangent.reshape(field.shape)
    factor = 1.0 / (MB * IMG * SIDE * SIDE)
    grads_in = [None] * SECTIONS
    input_grads = [None] * SECTIONS
    for section in range(SECTIONS - 1, -1, -1):
        input_grad, flat, pre_grad = block_backward(kept[section], upstream, dw_kernel[section], layer_scale[section], w_in[section], w_out[section])
        grads_in[section] = jnp.dot(pre_grad.T, flat, preferred_element_type=jnp.float32) * factor
        input_grads[section] = input_grad.reshape(images.shape)
        upstream = input_grad
    return (jnp.stack(grads_in), jnp.stack(input_grads))
```

```python
import jax
import jax.numpy as jnp
from jax import lax
from jax.sharding import PartitionSpec as P

KS = 7


EPS = 1e-06


def shifted(block, axis, distance):
    devices = range(lax.axis_size(axis))
    route = [(i - distance, i) for i in devices if i - distance in devices]
    return lax.ppermute(block, axis, route)


def depthwise(field, kernel):
    reach = KS // 2
    height = field.shape[1]
    padded = jnp.pad(field, ((0, 0), (reach, reach), (reach, reach), (0, 0)))
    total = jnp.zeros(field.shape, jnp.float32)
    for row in range(KS):
        for col in range(KS):
            total = (
                total
                + padded[:, row : row + height, col : col + height, :] * kernel[row * KS + col]
            )
    return total


def depthwise_adjoint(field, kernel):
    reach = KS // 2
    height = field.shape[1]
    padded = jnp.pad(field, ((0, 0), (reach, reach), (reach, reach), (0, 0)))
    total = jnp.zeros(field.shape, jnp.float32)
    for row in range(KS):
        for col in range(KS):
            top = 2 * reach - row
            left = 2 * reach - col
            total = (
                total
                + padded[:, top : top + height, left : left + height, :] * kernel[row * KS + col]
            )
    return total


def gelu_parts(value):
    normal_cdf = 0.5 * (1.0 + lax.erf(value * 0.7071067811865476))
    density = jnp.exp(-0.5 * value * value) * 0.3989422804014327
    return (value * normal_cdf, normal_cdf + value * density)


def block_inner(inputs, kernel, weight_in):
    width = inputs.shape[-1]
    mixed = depthwise(inputs.astype(jnp.float32), kernel)
    center = mixed - jnp.mean(mixed, axis=-1, keepdims=True)
    inv_std = lax.rsqrt(jnp.mean(center * center, axis=-1, keepdims=True) + EPS)
    normed = center * inv_std
    flat = normed.reshape(-1, width).astype(jnp.bfloat16)
    pre = lax.dot_general(
        flat, weight_in, (((1,), (1,)), ((), ())), preferred_element_type=jnp.float32
    )
    active, slope = gelu_parts(pre)
    hidden = active.astype(jnp.bfloat16)
    return (normed, inv_std, flat, slope, hidden)


def block_forward(inputs, kernel, scale, weight_in, weight_out):
    width = inputs.shape[-1]
    normed, inv_std, flat, slope, hidden = block_inner(inputs, kernel, weight_in)
    branch = jnp.dot(hidden, weight_out, preferred_element_type=jnp.float32)
    output = inputs.reshape(-1, width).astype(jnp.float32) + scale * branch
    return output.astype(jnp.bfloat16).reshape(inputs.shape)


def block_backward(inputs, upstream, kernel, scale, weight_in, weight_out):
    width = inputs.shape[-1]
    normed, inv_std, flat, slope, hidden = block_inner(inputs, kernel, weight_in)
    up_flat = upstream.reshape(-1, width).astype(jnp.float32)
    branch_grad = (scale * up_flat).astype(jnp.bfloat16)
    hidden_grad = lax.dot_general(
        branch_grad, weight_out, (((1,), (1,)), ((), ())), preferred_element_type=jnp.float32
    )
    pre_grad = (hidden_grad * slope).astype(jnp.bfloat16)
    normed_grad = jnp.dot(pre_grad, weight_in, preferred_element_type=jnp.float32).reshape(
        inputs.shape
    )
    mean_grad = jnp.mean(normed_grad, axis=-1, keepdims=True)
    mean_cross = jnp.mean(normed_grad * normed, axis=-1, keepdims=True)
    mixed_grad = inv_std * (normed_grad - mean_grad - normed * mean_cross)
    input_grad = (upstream.astype(jnp.float32) + depthwise_adjoint(mixed_grad, kernel)).astype(
        jnp.bfloat16
    )
    return (input_grad, flat, pre_grad)


def place(buffer, value, slot, active):
    former = lax.dynamic_index_in_dim(buffer, slot, 0, keepdims=False)
    return lax.dynamic_update_index_in_dim(buffer, jnp.where(active, value, former), slot, 0)


def body(images, cotangent, dw_kernel, layer_scale, w_in, w_out):
    section = lax.axis_index("section")
    sections = lax.axis_size("section")
    micro_count, img_count, side, _, width = images.shape
    kernel = dw_kernel[0]
    scale = layer_scale[0]
    weight_in = w_in[0]
    weight_out = w_out[0]
    hidden_width = weight_in.shape[0]
    pixel_rows = img_count * side * side
    ticks = micro_count + sections - 1
    factor = 1.0 / (micro_count * pixel_rows)
    blank = jnp.zeros(images.shape[1:], jnp.bfloat16)

    def run_forward(entering):
        return block_forward(entering, kernel, scale, weight_in, weight_out)

    def skip_forward(entering):
        return jnp.zeros_like(entering)

    def forward_tick(tick, carry):
        incoming, kept = carry
        micro = tick - section
        active = (micro >= 0) & (micro < micro_count)
        slot = jnp.clip(micro, 0, micro_count - 1)
        own = lax.dynamic_index_in_dim(images, slot, 0, keepdims=False)
        entering = jnp.where(section == 0, own, incoming)
        leaving = lax.cond(active, run_forward, skip_forward, entering)
        kept = place(kept, entering, slot, active)
        incoming = shifted(leaving, "section", 1)
        return (incoming, kept)

    _, kept = lax.fori_loop(0, ticks, forward_tick, (blank, jnp.zeros(images.shape, jnp.bfloat16)))

    def run_backward(entering, upstream):
        return block_backward(entering, upstream, kernel, scale, weight_in, weight_out)

    def skip_backward(entering, upstream):
        return (
            jnp.zeros_like(upstream),
            jnp.zeros((pixel_rows, width), jnp.bfloat16),
            jnp.zeros((pixel_rows, hidden_width), jnp.bfloat16),
        )

    stores = (
        jnp.zeros((micro_count, pixel_rows, width), jnp.bfloat16),
        jnp.zeros((micro_count, pixel_rows, hidden_width), jnp.bfloat16),
    )
    summed = jnp.zeros((1,), jnp.float32)

    def backward_tick(tick, carry):
        incoming, grads, stored, total = carry
        micro = tick - (sections - 1 - section)
        active = (micro >= 0) & (micro < micro_count)
        slot = jnp.clip(micro, 0, micro_count - 1)
        own = lax.dynamic_index_in_dim(cotangent, slot, 0, keepdims=False)
        upstream = jnp.where(section == sections - 1, own, incoming)
        entering = lax.dynamic_index_in_dim(kept, slot, 0, keepdims=False)
        input_grad, flat, pre_grad = lax.cond(
            active, run_backward, skip_backward, entering, upstream
        )
        grads = place(grads, input_grad, slot, active)
        stored = (place(stored[0], flat, slot, active), place(stored[1], pre_grad, slot, active))
        incoming = shifted(input_grad, "section", -1)
        return (incoming, grads, stored, total)

    _, grads, stores, summed = lax.fori_loop(
        0, ticks, backward_tick, (blank, jnp.zeros(images.shape, jnp.bfloat16), stores, summed)
    )
    all_flat = stores[0].reshape(micro_count * pixel_rows, width)
    all_pre = stores[1].reshape(micro_count * pixel_rows, hidden_width)
    partial = (
        lax.dot_general(
            all_pre, all_flat, (((0,), (0,)), ((), ())), preferred_element_type=jnp.float32
        )
        * factor
    )
    replicas = lax.axis_size("dp")
    share = (hidden_width // replicas) * width
    padded = -(-share // 1024) * 1024
    chunks = jnp.pad(partial.reshape(replicas, share), ((0, 0), (0, padded - share)))
    mine = lax.psum_scatter(
        chunks.reshape(replicas, padded // 128, 128), "dp", scatter_dimension=0, tiled=True
    )
    sums = mine.reshape(padded)[:share].reshape(hidden_width // replicas, width)
    return (sums[None], grads[None])


def solution(mesh):
    return jax.shard_map(
        body,
        mesh=mesh,
        in_specs=(
            P(None, "dp", None, None, None),
            P(None, "dp", None, None, None),
            P("section", None, None),
            P("section", None),
            P("section", None, None),
            P("section", None, None),
        ),
        out_specs=(P("section", "dp", None), P("section", None, "dp", None, None, None)),
        check_vma=False,
    )
```

```python
import jax
import jax.numpy as jnp
from jax import lax
from jax.sharding import Mesh, PartitionSpec as P

KS = 7


EPS = 1e-06


def shifted(block, axis, distance):
    devices = range(lax.axis_size(axis))
    route = [(i - distance, i) for i in devices if i - distance in devices]
    return lax.ppermute(block, axis, route)


def depthwise(field, kernel):
    reach = KS // 2
    height = field.shape[1]
    padded = jnp.pad(field, ((0, 0), (reach, reach), (reach, reach), (0, 0)))
    total = jnp.zeros(field.shape, jnp.float32)
    for row in range(KS):
        for col in range(KS):
            total = (
                total
                + padded[:, row : row + height, col : col + height, :] * kernel[row * KS + col]
            )
    return total


def depthwise_adjoint(field, kernel):
    reach = KS // 2
    height = field.shape[1]
    padded = jnp.pad(field, ((0, 0), (reach, reach), (reach, reach), (0, 0)))
    total = jnp.zeros(field.shape, jnp.float32)
    for row in range(KS):
        for col in range(KS):
            top = 2 * reach - row
            left = 2 * reach - col
            total = (
                total
                + padded[:, top : top + height, left : left + height, :] * kernel[row * KS + col]
            )
    return total


def gelu_parts(value):
    normal_cdf = 0.5 * (1.0 + lax.erf(value * 0.7071067811865476))
    density = jnp.exp(-0.5 * value * value) * 0.3989422804014327
    return (value * normal_cdf, normal_cdf + value * density)


def block_inner(inputs, kernel, weight_in):
    width = inputs.shape[-1]
    mixed = depthwise(inputs.astype(jnp.float32), kernel)
    center = mixed - jnp.mean(mixed, axis=-1, keepdims=True)
    inv_std = lax.rsqrt(jnp.mean(center * center, axis=-1, keepdims=True) + EPS)
    normed = center * inv_std
    flat = normed.reshape(-1, width).astype(jnp.bfloat16)
    pre = lax.dot_general(
        flat, weight_in, (((1,), (1,)), ((), ())), preferred_element_type=jnp.float32
    )
    active, slope = gelu_parts(pre)
    hidden = active.astype(jnp.bfloat16)
    return (normed, inv_std, flat, slope, hidden)


def block_forward(inputs, kernel, scale, weight_in, weight_out):
    width = inputs.shape[-1]
    normed, inv_std, flat, slope, hidden = block_inner(inputs, kernel, weight_in)
    branch = jnp.dot(hidden, weight_out, preferred_element_type=jnp.float32)
    output = inputs.reshape(-1, width).astype(jnp.float32) + scale * branch
    return output.astype(jnp.bfloat16).reshape(inputs.shape)


def block_backward(inputs, upstream, kernel, scale, weight_in, weight_out):
    width = inputs.shape[-1]
    normed, inv_std, flat, slope, hidden = block_inner(inputs, kernel, weight_in)
    up_flat = upstream.reshape(-1, width).astype(jnp.float32)
    branch_grad = (scale * up_flat).astype(jnp.bfloat16)
    hidden_grad = lax.dot_general(
        branch_grad, weight_out, (((1,), (1,)), ((), ())), preferred_element_type=jnp.float32
    )
    pre_grad = (hidden_grad * slope).astype(jnp.bfloat16)
    normed_grad = jnp.dot(pre_grad, weight_in, preferred_element_type=jnp.float32).reshape(
        inputs.shape
    )
    mean_grad = jnp.mean(normed_grad, axis=-1, keepdims=True)
    mean_cross = jnp.mean(normed_grad * normed, axis=-1, keepdims=True)
    mixed_grad = inv_std * (normed_grad - mean_grad - normed * mean_cross)
    input_grad = (upstream.astype(jnp.float32) + depthwise_adjoint(mixed_grad, kernel)).astype(
        jnp.bfloat16
    )
    return (input_grad, flat, pre_grad)


def place(buffer, value, micro, count):
    slot = jnp.clip(micro, -1, count) + 1
    return lax.dynamic_update_index_in_dim(buffer, value, slot, 0)


def body(images, cotangent, dw_kernel, layer_scale, w_in, w_out):
    section = lax.axis_index("section")
    sections = lax.axis_size("section")
    micro_count, img_count, side, _, width = images.shape
    kernel = dw_kernel[0]
    scale = layer_scale[0]
    weight_in = w_in[0]
    weight_out = w_out[0]
    hidden_width = weight_in.shape[0]
    pixel_rows = img_count * side * side
    ticks = micro_count + sections - 1
    factor = 1.0 / (micro_count * pixel_rows)
    blank = jnp.zeros(images.shape[1:], jnp.bfloat16)

    def run_forward(entering):
        return block_forward(entering, kernel, scale, weight_in, weight_out)

    def skip_forward(entering):
        return jnp.zeros_like(entering)

    def forward_tick(tick, carry):
        incoming, kept = carry
        micro = tick - section
        active = (micro >= 0) & (micro < micro_count)
        slot = jnp.clip(micro, 0, micro_count - 1)
        own = lax.dynamic_index_in_dim(images, slot, 0, keepdims=False)
        entering = jnp.where(section == 0, own, incoming)
        leaving = lax.cond(active, run_forward, skip_forward, entering)
        kept = place(kept, entering, micro, micro_count)
        incoming = shifted(leaving, "section", 1)
        return (incoming, kept)

    spare = (micro_count + 2,) + images.shape[1:]
    _, kept = lax.fori_loop(0, ticks, forward_tick, (blank, jnp.zeros(spare, jnp.bfloat16)))

    def run_backward(entering, upstream):
        return block_backward(entering, upstream, kernel, scale, weight_in, weight_out)

    def skip_backward(entering, upstream):
        return (
            jnp.zeros_like(upstream),
            jnp.zeros((pixel_rows, width), jnp.bfloat16),
            jnp.zeros((pixel_rows, hidden_width), jnp.bfloat16),
        )

    stores = (
        jnp.zeros((micro_count + 2, pixel_rows, width), jnp.bfloat16),
        jnp.zeros((micro_count + 2, pixel_rows, hidden_width), jnp.bfloat16),
    )
    summed = jnp.zeros((1,), jnp.float32)

    def backward_tick(tick, carry):
        incoming, grads, stored, total = carry
        micro = tick - (sections - 1 - section)
        active = (micro >= 0) & (micro < micro_count)
        slot = jnp.clip(micro, 0, micro_count - 1)
        own = lax.dynamic_index_in_dim(cotangent, slot, 0, keepdims=False)
        upstream = jnp.where(section == sections - 1, own, incoming)
        entering = lax.dynamic_index_in_dim(kept, slot + 1, 0, keepdims=False)
        input_grad, flat, pre_grad = lax.cond(
            active, run_backward, skip_backward, entering, upstream
        )
        grads = place(grads, input_grad, micro, micro_count)
        stored = (
            place(stored[0], flat, micro, micro_count),
            place(stored[1], pre_grad, micro, micro_count),
        )
        incoming = shifted(input_grad, "section", -1)
        return (incoming, grads, stored, total)

    _, grads, stores, summed = lax.fori_loop(
        0, ticks, backward_tick, (blank, jnp.zeros(spare, jnp.bfloat16), stores, summed)
    )
    grads = grads[1 : micro_count + 1]
    all_flat = stores[0][1 : micro_count + 1].reshape(micro_count * pixel_rows, width)
    all_pre = stores[1][1 : micro_count + 1].reshape(micro_count * pixel_rows, hidden_width)
    partial = (
        lax.dot_general(
            all_pre, all_flat, (((0,), (0,)), ((), ())), preferred_element_type=jnp.float32
        )
        * factor
    )
    cores, rows, planes = (lax.axis_size(name) for name in ("core", "y", "z"))
    replicas = cores * rows * planes
    share = (hidden_width // replicas) * width
    padded = -(-share // 1024) * 1024
    chunks = jnp.pad(partial.reshape(replicas, share), ((0, 0), (0, padded - share)))
    mine = lax.psum_scatter(
        chunks.reshape(replicas, padded // 128, 128), ("z", "y", "core"), scatter_dimension=0, tiled=True
    )
    sums = mine.reshape(padded)[:share].reshape(hidden_width // replicas, width)
    return (sums[None], grads[None])


def solution(mesh):
    sections, replicas = mesh.devices.shape
    cores = 2
    rows = int(round((replicas // cores) ** 0.5))
    split = Mesh(
        mesh.devices.reshape(sections, replicas // (rows * cores), rows, cores),
        ("section", "z", "y", "core"),
    )
    dp = ("z", "y", "core")
    return jax.shard_map(
        body,
        mesh=split,
        in_specs=(
            P(None, dp, None, None, None),
            P(None, dp, None, None, None),
            P("section", None, None),
            P("section", None),
            P("section", None, None),
            P("section", None, None),
        ),
        out_specs=(P("section", dp, None), P("section", None, dp, None, None, None)),
        check_vma=False,
    )
```

```python
import jax
import jax.numpy as jnp
from jax import lax
from jax.sharding import Mesh, PartitionSpec as P

KS = 7


EPS = 1e-06


def shifted(block, axis, distance):
    devices = range(lax.axis_size(axis))
    route = [(i - distance, i) for i in devices if i - distance in devices]
    return lax.ppermute(block, axis, route)


def depthwise(field, kernel):
    reach = KS // 2
    height = field.shape[1]
    padded = jnp.pad(field, ((0, 0), (reach, reach), (reach, reach), (0, 0)))
    total = jnp.zeros(field.shape, jnp.float32)
    for row in range(KS):
        for col in range(KS):
            total = (
                total
                + padded[:, row : row + height, col : col + height, :] * kernel[row * KS + col]
            )
    return total


def depthwise_adjoint(field, kernel):
    reach = KS // 2
    height = field.shape[1]
    padded = jnp.pad(field, ((0, 0), (reach, reach), (reach, reach), (0, 0)))
    total = jnp.zeros(field.shape, jnp.float32)
    for row in range(KS):
        for col in range(KS):
            top = 2 * reach - row
            left = 2 * reach - col
            total = (
                total
                + padded[:, top : top + height, left : left + height, :] * kernel[row * KS + col]
            )
    return total


def gelu_parts(value):
    normal_cdf = 0.5 * (1.0 + lax.erf(value * 0.7071067811865476))
    density = jnp.exp(-0.5 * value * value) * 0.3989422804014327
    return (value * normal_cdf, normal_cdf + value * density)


def block_inner(inputs, kernel, weight_in):
    width = inputs.shape[-1]
    mixed = depthwise(inputs.astype(jnp.float32), kernel)
    center = mixed - jnp.mean(mixed, axis=-1, keepdims=True)
    inv_std = lax.rsqrt(jnp.mean(center * center, axis=-1, keepdims=True) + EPS)
    normed = center * inv_std
    flat = normed.reshape(-1, width).astype(jnp.bfloat16)
    pre = lax.dot_general(
        flat, weight_in, (((1,), (1,)), ((), ())), preferred_element_type=jnp.float32
    )
    active, slope = gelu_parts(pre)
    hidden = active.astype(jnp.bfloat16)
    return (normed, inv_std, flat, slope, hidden)


def block_forward(inputs, kernel, scale, weight_in, weight_out):
    width = inputs.shape[-1]
    normed, inv_std, flat, slope, hidden = block_inner(inputs, kernel, weight_in)
    branch = jnp.dot(hidden, weight_out, preferred_element_type=jnp.float32)
    output = inputs.reshape(-1, width).astype(jnp.float32) + scale * branch
    return output.astype(jnp.bfloat16).reshape(inputs.shape)


def block_backward(inputs, upstream, kernel, scale, weight_in, weight_out):
    width = inputs.shape[-1]
    normed, inv_std, flat, slope, hidden = block_inner(inputs, kernel, weight_in)
    up_flat = upstream.reshape(-1, width).astype(jnp.float32)
    branch_grad = (scale * up_flat).astype(jnp.bfloat16)
    hidden_grad = lax.dot_general(
        branch_grad, weight_out, (((1,), (1,)), ((), ())), preferred_element_type=jnp.float32
    )
    pre_grad = (hidden_grad * slope).astype(jnp.bfloat16)
    normed_grad = jnp.dot(pre_grad, weight_in, preferred_element_type=jnp.float32).reshape(
        inputs.shape
    )
    mean_grad = jnp.mean(normed_grad, axis=-1, keepdims=True)
    mean_cross = jnp.mean(normed_grad * normed, axis=-1, keepdims=True)
    mixed_grad = inv_std * (normed_grad - mean_grad - normed * mean_cross)
    input_grad = (upstream.astype(jnp.float32) + depthwise_adjoint(mixed_grad, kernel)).astype(
        jnp.bfloat16
    )
    return (input_grad, flat, pre_grad)


def place(buffer, value, micro, count):
    slot = jnp.clip(micro, -1, count) + 1
    return lax.dynamic_update_index_in_dim(buffer, value, slot, 0)


def halve(chunks, axis, bit):
    mine = (lax.axis_index(axis) // bit) % 2
    pairs = chunks.reshape((chunks.shape[0] // 2, 2) + chunks.shape[1:])
    keep = lax.dynamic_index_in_dim(pairs, mine, 1, keepdims=False)
    send = lax.dynamic_index_in_dim(pairs, 1 - mine, 1, keepdims=False)
    route = [(i, i ^ bit) for i in range(lax.axis_size(axis))]
    return keep + lax.ppermute(send, axis, route)


def body(images, cotangent, dw_kernel, layer_scale, w_in, w_out):
    section = lax.axis_index("section")
    sections = lax.axis_size("section")
    micro_count, img_count, side, _, width = images.shape
    kernel = dw_kernel[0]
    scale = layer_scale[0]
    weight_in = w_in[0]
    weight_out = w_out[0]
    hidden_width = weight_in.shape[0]
    pixel_rows = img_count * side * side
    ticks = micro_count + sections - 1
    factor = 1.0 / (micro_count * pixel_rows)
    blank = jnp.zeros(images.shape[1:], jnp.bfloat16)

    def run_forward(entering):
        return block_forward(entering, kernel, scale, weight_in, weight_out)

    def skip_forward(entering):
        return jnp.zeros_like(entering)

    def forward_tick(tick, carry):
        incoming, kept = carry
        micro = tick - section
        active = (micro >= 0) & (micro < micro_count)
        slot = jnp.clip(micro, 0, micro_count - 1)
        own = lax.dynamic_index_in_dim(images, slot, 0, keepdims=False)
        entering = jnp.where(section == 0, own, incoming)
        leaving = lax.cond(active, run_forward, skip_forward, entering)
        kept = place(kept, entering, micro, micro_count)
        incoming = shifted(leaving, "section", 1)
        return (incoming, kept)

    spare = (micro_count + 2,) + images.shape[1:]
    _, kept = lax.fori_loop(0, ticks, forward_tick, (blank, jnp.zeros(spare, jnp.bfloat16)))

    def run_backward(entering, upstream):
        return block_backward(entering, upstream, kernel, scale, weight_in, weight_out)

    def skip_backward(entering, upstream):
        return (
            jnp.zeros_like(upstream),
            jnp.zeros((pixel_rows, width), jnp.bfloat16),
            jnp.zeros((pixel_rows, hidden_width), jnp.bfloat16),
        )

    stores = (
        jnp.zeros((micro_count + 2, pixel_rows, width), jnp.bfloat16),
        jnp.zeros((micro_count + 2, pixel_rows, hidden_width), jnp.bfloat16),
    )
    summed = jnp.zeros((1,), jnp.float32)

    def backward_tick(tick, carry):
        incoming, grads, stored, total = carry
        micro = tick - (sections - 1 - section)
        active = (micro >= 0) & (micro < micro_count)
        slot = jnp.clip(micro, 0, micro_count - 1)
        own = lax.dynamic_index_in_dim(cotangent, slot, 0, keepdims=False)
        upstream = jnp.where(section == sections - 1, own, incoming)
        entering = lax.dynamic_index_in_dim(kept, slot + 1, 0, keepdims=False)
        input_grad, flat, pre_grad = lax.cond(
            active, run_backward, skip_backward, entering, upstream
        )
        grads = place(grads, input_grad, micro, micro_count)
        stored = (
            place(stored[0], flat, micro, micro_count),
            place(stored[1], pre_grad, micro, micro_count),
        )
        incoming = shifted(input_grad, "section", -1)
        return (incoming, grads, stored, total)

    _, grads, stores, summed = lax.fori_loop(
        0, ticks, backward_tick, (blank, jnp.zeros(spare, jnp.bfloat16), stores, summed)
    )
    grads = grads[1 : micro_count + 1]
    all_flat = stores[0][1 : micro_count + 1].reshape(micro_count * pixel_rows, width)
    all_pre = stores[1][1 : micro_count + 1].reshape(micro_count * pixel_rows, hidden_width)
    partial = (
        lax.dot_general(
            all_pre, all_flat, (((0,), (0,)), ((), ())), preferred_element_type=jnp.float32
        )
        * factor
    )
    replicas = 1
    for name in ("z", "y", "core"):
        replicas *= lax.axis_size(name)
    share = (hidden_width // replicas) * width
    padded = -(-share // 1024) * 1024
    chunks = jnp.pad(partial.reshape(replicas, share), ((0, 0), (0, padded - share)))
    chunks = chunks.reshape(replicas, padded // 128, 128)
    for name in ("core", "y", "z"):
        bit = 1
        while bit < lax.axis_size(name):
            chunks = halve(chunks, name, bit)
            bit *= 2
    sums = chunks.reshape(padded)[:share].reshape(hidden_width // replicas, width)
    return (sums[None], grads[None])


def solution(mesh):
    sections, replicas = mesh.devices.shape
    cores = 2
    rows = int(round((replicas // cores) ** 0.5))
    split = Mesh(
        mesh.devices.reshape(sections, replicas // (rows * cores), rows, cores),
        ("section", "z", "y", "core"),
    )
    dp = ("z", "y", "core")
    return jax.shard_map(
        body,
        mesh=split,
        in_specs=(
            P(None, dp, None, None, None),
            P(None, dp, None, None, None),
            P("section", None, None),
            P("section", None),
            P("section", None, None),
            P("section", None, None),
        ),
        out_specs=(P("section", dp, None), P("section", None, dp, None, None, None)),
        check_vma=False,
    )
```

```python
import jax
import jax.numpy as jnp
from jax import lax
from jax.sharding import Mesh, PartitionSpec as P

KS = 7


EPS = 1e-06


def shifted(block, axis, distance):
    devices = range(lax.axis_size(axis))
    route = [(i - distance, i) for i in devices if i - distance in devices]
    return lax.ppermute(block, axis, route)


def depthwise(field, kernel):
    reach = KS // 2
    height = field.shape[1]
    padded = jnp.pad(field, ((0, 0), (reach, reach), (reach, reach), (0, 0)))
    total = jnp.zeros(field.shape, jnp.float32)
    for row in range(KS):
        for col in range(KS):
            total = (
                total
                + padded[:, row : row + height, col : col + height, :] * kernel[row * KS + col]
            )
    return total


def depthwise_adjoint(field, kernel):
    reach = KS // 2
    height = field.shape[1]
    padded = jnp.pad(field, ((0, 0), (reach, reach), (reach, reach), (0, 0)))
    total = jnp.zeros(field.shape, jnp.float32)
    for row in range(KS):
        for col in range(KS):
            top = 2 * reach - row
            left = 2 * reach - col
            total = (
                total
                + padded[:, top : top + height, left : left + height, :] * kernel[row * KS + col]
            )
    return total


def gelu_parts(value):
    normal_cdf = 0.5 * (1.0 + lax.erf(value * 0.7071067811865476))
    density = jnp.exp(-0.5 * value * value) * 0.3989422804014327
    return (value * normal_cdf, normal_cdf + value * density)


def block_inner(inputs, kernel, weight_in):
    width = inputs.shape[-1]
    mixed = depthwise(inputs.astype(jnp.float32), kernel)
    center = mixed - jnp.mean(mixed, axis=-1, keepdims=True)
    inv_std = lax.rsqrt(jnp.mean(center * center, axis=-1, keepdims=True) + EPS)
    normed = center * inv_std
    flat = normed.reshape(-1, width).astype(jnp.bfloat16)
    pre = lax.dot_general(
        flat, weight_in, (((1,), (1,)), ((), ())), preferred_element_type=jnp.float32
    )
    active, slope = gelu_parts(pre)
    hidden = active.astype(jnp.bfloat16)
    return (normed, inv_std, flat, slope, hidden)


def block_forward(inputs, kernel, scale, weight_in, weight_out):
    width = inputs.shape[-1]
    normed, inv_std, flat, slope, hidden = block_inner(inputs, kernel, weight_in)
    branch = jnp.dot(hidden, weight_out, preferred_element_type=jnp.float32)
    output = inputs.reshape(-1, width).astype(jnp.float32) + scale * branch
    return output.astype(jnp.bfloat16).reshape(inputs.shape)


def block_backward(inputs, upstream, kernel, scale, weight_in, weight_out):
    width = inputs.shape[-1]
    normed, inv_std, flat, slope, hidden = block_inner(inputs, kernel, weight_in)
    up_flat = upstream.reshape(-1, width).astype(jnp.float32)
    branch_grad = (scale * up_flat).astype(jnp.bfloat16)
    hidden_grad = lax.dot_general(
        branch_grad, weight_out, (((1,), (1,)), ((), ())), preferred_element_type=jnp.float32
    )
    pre_grad = (hidden_grad * slope).astype(jnp.bfloat16)
    normed_grad = jnp.dot(pre_grad, weight_in, preferred_element_type=jnp.float32).reshape(
        inputs.shape
    )
    mean_grad = jnp.mean(normed_grad, axis=-1, keepdims=True)
    mean_cross = jnp.mean(normed_grad * normed, axis=-1, keepdims=True)
    mixed_grad = inv_std * (normed_grad - mean_grad - normed * mean_cross)
    input_grad = (upstream.astype(jnp.float32) + depthwise_adjoint(mixed_grad, kernel)).astype(
        jnp.bfloat16
    )
    return (input_grad, flat, pre_grad)


def place(buffer, value, micro, count):
    slot = jnp.clip(micro, -1, count) + 1
    return lax.dynamic_update_index_in_dim(buffer, value, slot, 0)


def halve(chunks, axis, bit):
    mine = (lax.axis_index(axis) // bit) % 2
    pairs = chunks.reshape((chunks.shape[0] // 2, 2) + chunks.shape[1:])
    keep = lax.dynamic_index_in_dim(pairs, mine, 1, keepdims=False)
    send = lax.dynamic_index_in_dim(pairs, 1 - mine, 1, keepdims=False)
    route = [(i, i ^ bit) for i in range(lax.axis_size(axis))]
    return keep + lax.ppermute(send, axis, route)


def body(images, cotangent, dw_kernel, layer_scale, w_in, w_out):
    section = lax.axis_index("section")
    sections = lax.axis_size("section")
    micro_count, img_count, side, _, width = images.shape
    kernel = lax.optimization_barrier(tuple(dw_kernel[0, tap] for tap in range(KS * KS)))
    scale = layer_scale[0]
    weight_in = w_in[0]
    weight_out = w_out[0]
    hidden_width = weight_in.shape[0]
    pixel_rows = img_count * side * side
    ticks = micro_count + sections - 1
    factor = 1.0 / (micro_count * pixel_rows)
    blank = jnp.zeros(images.shape[1:], jnp.bfloat16)

    def run_forward(entering):
        return block_forward(entering, kernel, scale, weight_in, weight_out)

    def forward_tick(tick, carry):
        incoming, kept = carry
        micro = tick - section
        slot = jnp.clip(micro, 0, micro_count - 1)
        own = lax.dynamic_index_in_dim(images, slot, 0, keepdims=False)
        entering = jnp.where(section == 0, own, incoming)
        leaving = run_forward(entering)
        kept = place(kept, entering, micro, micro_count)
        incoming = shifted(leaving, "section", 1)
        return (incoming, kept)

    spare = (micro_count + 2,) + images.shape[1:]
    _, kept = lax.fori_loop(0, ticks, forward_tick, (blank, jnp.zeros(spare, jnp.bfloat16)))

    def run_backward(entering, upstream):
        return block_backward(entering, upstream, kernel, scale, weight_in, weight_out)

    stores = (
        jnp.zeros((micro_count + 2, pixel_rows, width), jnp.bfloat16),
        jnp.zeros((micro_count + 2, pixel_rows, hidden_width), jnp.bfloat16),
    )
    summed = jnp.zeros((1,), jnp.float32)

    def backward_tick(tick, carry):
        incoming, grads, stored, total = carry
        micro = tick - (sections - 1 - section)
        slot = jnp.clip(micro, 0, micro_count - 1)
        own = lax.dynamic_index_in_dim(cotangent, slot, 0, keepdims=False)
        upstream = jnp.where(section == sections - 1, own, incoming)
        entering = lax.dynamic_index_in_dim(kept, slot + 1, 0, keepdims=False)
        input_grad, flat, pre_grad = run_backward(entering, upstream)
        grads = place(grads, input_grad, micro, micro_count)
        stored = (
            place(stored[0], flat, micro, micro_count),
            place(stored[1], pre_grad, micro, micro_count),
        )
        incoming = shifted(input_grad, "section", -1)
        return (incoming, grads, stored, total)

    _, grads, stores, summed = lax.fori_loop(
        0, ticks, backward_tick, (blank, jnp.zeros(spare, jnp.bfloat16), stores, summed)
    )
    grads = grads[1 : micro_count + 1]
    all_flat = stores[0][1 : micro_count + 1].reshape(micro_count * pixel_rows, width)
    all_pre = stores[1][1 : micro_count + 1].reshape(micro_count * pixel_rows, hidden_width)
    partial = (
        lax.dot_general(
            all_pre, all_flat, (((0,), (0,)), ((), ())), preferred_element_type=jnp.float32
        )
        * factor
    )
    replicas = 1
    for name in ("z", "y", "core"):
        replicas *= lax.axis_size(name)
    share = (hidden_width // replicas) * width
    padded = -(-share // 1024) * 1024
    chunks = jnp.pad(partial.reshape(replicas, share), ((0, 0), (0, padded - share)))
    chunks = chunks.reshape(replicas, padded // 128, 128)
    for name in ("core", "y", "z"):
        bit = 1
        while bit < lax.axis_size(name):
            chunks = halve(chunks, name, bit)
            bit *= 2
    sums = chunks.reshape(padded)[:share].reshape(hidden_width // replicas, width)
    return (sums[None], grads[None])


def solution(mesh):
    sections, replicas = mesh.devices.shape
    cores = 2
    rows = int(round((replicas // cores) ** 0.5))
    split = Mesh(
        mesh.devices.reshape(sections, replicas // (rows * cores), rows, cores),
        ("section", "z", "y", "core"),
    )
    dp = ("z", "y", "core")
    return jax.shard_map(
        body,
        mesh=split,
        in_specs=(
            P(None, dp, None, None, None),
            P(None, dp, None, None, None),
            P("section", None, None),
            P("section", None),
            P("section", None, None),
            P("section", None, None),
        ),
        out_specs=(P("section", dp, None), P("section", None, dp, None, None, None)),
        check_vma=False,
    )
```

```python
import jax
import jax.numpy as jnp
from jax import lax
from jax.sharding import Mesh, PartitionSpec as P

KS = 7


EPS = 1e-06


def shifted(block, axis, distance):
    devices = range(lax.axis_size(axis))
    route = [(i - distance, i) for i in devices if i - distance in devices]
    return lax.ppermute(block, axis, route)


def depthwise(field, kernel):
    reach = KS // 2
    height = field.shape[1]
    padded = jnp.pad(field, ((0, 0), (reach, reach), (reach, reach), (0, 0)))
    total = jnp.zeros(field.shape, jnp.float32)
    for row in range(KS):
        for col in range(KS):
            total = (
                total
                + padded[:, row : row + height, col : col + height, :] * kernel[row * KS + col]
            )
    return total


def depthwise_adjoint(field, kernel):
    reach = KS // 2
    height = field.shape[1]
    padded = jnp.pad(field, ((0, 0), (reach, reach), (reach, reach), (0, 0)))
    total = jnp.zeros(field.shape, jnp.float32)
    for row in range(KS):
        for col in range(KS):
            top = 2 * reach - row
            left = 2 * reach - col
            total = (
                total
                + padded[:, top : top + height, left : left + height, :] * kernel[row * KS + col]
            )
    return total


def gelu_parts(value):
    normal_cdf = 0.5 * (1.0 + lax.erf(value * 0.7071067811865476))
    density = jnp.exp(-0.5 * value * value) * 0.3989422804014327
    return (value * normal_cdf, normal_cdf + value * density)


def block_inner(inputs, kernel, weight_in):
    width = inputs.shape[-1]
    mixed = depthwise(inputs.astype(jnp.float32), kernel)
    center = mixed - jnp.mean(mixed, axis=-1, keepdims=True)
    inv_std = lax.rsqrt(jnp.mean(center * center, axis=-1, keepdims=True) + EPS)
    normed = center * inv_std
    flat = normed.reshape(-1, width).astype(jnp.bfloat16)
    pre = lax.dot_general(
        flat, weight_in, (((1,), (1,)), ((), ())), preferred_element_type=jnp.float32
    )
    active, slope = gelu_parts(pre)
    hidden = active.astype(jnp.bfloat16)
    return (normed, inv_std, flat, slope, hidden)


def block_forward(inputs, kernel, scale, weight_in, weight_out):
    width = inputs.shape[-1]
    normed, inv_std, flat, slope, hidden = block_inner(inputs, kernel, weight_in)
    branch = jnp.dot(hidden, weight_out, preferred_element_type=jnp.float32)
    output = inputs.reshape(-1, width).astype(jnp.float32) + scale * branch
    return output.astype(jnp.bfloat16).reshape(inputs.shape)


def block_forward_saving(inputs, kernel, scale, weight_in, weight_out):
    width = inputs.shape[-1]
    normed, inv_std, flat, slope, hidden = block_inner(inputs, kernel, weight_in)
    branch = jnp.dot(hidden, weight_out, preferred_element_type=jnp.float32)
    output = inputs.reshape(-1, width).astype(jnp.float32) + scale * branch
    return (output.astype(jnp.bfloat16).reshape(inputs.shape), normed, inv_std, slope)


def block_backward_saved(normed, inv_std, slope, upstream, kernel, scale, weight_in, weight_out):
    inputs = upstream
    width = inputs.shape[-1]
    flat = normed.reshape(-1, width).astype(jnp.bfloat16)
    up_flat = upstream.reshape(-1, width).astype(jnp.float32)
    branch_grad = (scale * up_flat).astype(jnp.bfloat16)
    hidden_grad = lax.dot_general(
        branch_grad, weight_out, (((1,), (1,)), ((), ())), preferred_element_type=jnp.float32
    )
    pre_grad = (hidden_grad * slope).astype(jnp.bfloat16)
    normed_grad = jnp.dot(pre_grad, weight_in, preferred_element_type=jnp.float32).reshape(
        inputs.shape
    )
    mean_grad = jnp.mean(normed_grad, axis=-1, keepdims=True)
    mean_cross = jnp.mean(normed_grad * normed, axis=-1, keepdims=True)
    mixed_grad = inv_std * (normed_grad - mean_grad - normed * mean_cross)
    input_grad = (upstream.astype(jnp.float32) + depthwise_adjoint(mixed_grad, kernel)).astype(
        jnp.bfloat16
    )
    return (input_grad, flat, pre_grad)


def place(buffer, value, micro, count):
    slot = jnp.clip(micro, -1, count) + 1
    return lax.dynamic_update_index_in_dim(buffer, value, slot, 0)


def halve(chunks, axis, bit):
    mine = (lax.axis_index(axis) // bit) % 2
    pairs = chunks.reshape((chunks.shape[0] // 2, 2) + chunks.shape[1:])
    keep = lax.dynamic_index_in_dim(pairs, mine, 1, keepdims=False)
    send = lax.dynamic_index_in_dim(pairs, 1 - mine, 1, keepdims=False)
    route = [(i, i ^ bit) for i in range(lax.axis_size(axis))]
    return keep + lax.ppermute(send, axis, route)


def body(images, cotangent, dw_kernel, layer_scale, w_in, w_out):
    section = lax.axis_index("section")
    sections = lax.axis_size("section")
    micro_count, img_count, side, _, width = images.shape
    kernel = lax.optimization_barrier(tuple(dw_kernel[0, tap] for tap in range(KS * KS)))
    scale = layer_scale[0]
    weight_in = w_in[0]
    weight_out = w_out[0]
    hidden_width = weight_in.shape[0]
    pixel_rows = img_count * side * side
    ticks = micro_count + sections - 1
    factor = 1.0 / (micro_count * pixel_rows)
    blank = jnp.zeros(images.shape[1:], jnp.bfloat16)

    def forward_tick(tick, carry):
        incoming, kept = carry
        micro = tick - section
        slot = jnp.clip(micro, 0, micro_count - 1)
        own = lax.dynamic_index_in_dim(images, slot, 0, keepdims=False)
        entering = jnp.where(section == 0, own, incoming)
        leaving, normed, inv_std, slope = block_forward_saving(
            entering, kernel, scale, weight_in, weight_out
        )
        kept = tuple(
            place(buffer, value, micro, micro_count)
            for buffer, value in zip(kept, (normed, inv_std, slope))
        )
        incoming = shifted(leaving, "section", 1)
        return (incoming, kept)

    spare = (micro_count + 2,) + images.shape[1:]
    kept = (
        jnp.zeros(spare, jnp.float32),
        jnp.zeros(spare[:-1] + (1,), jnp.float32),
        jnp.zeros((micro_count + 2, pixel_rows, hidden_width), jnp.float32),
    )
    _, kept = lax.fori_loop(0, ticks, forward_tick, (blank, kept))

    stores = jnp.zeros((micro_count + 2, pixel_rows, hidden_width), jnp.bfloat16)

    def backward_tick(tick, carry):
        incoming, grads, stored = carry
        micro = tick - (sections - 1 - section)
        slot = jnp.clip(micro, 0, micro_count - 1)
        own = lax.dynamic_index_in_dim(cotangent, slot, 0, keepdims=False)
        upstream = jnp.where(section == sections - 1, own, incoming)
        normed, inv_std, slope = (
            lax.dynamic_index_in_dim(buffer, slot + 1, 0, keepdims=False) for buffer in kept
        )
        input_grad, flat, pre_grad = block_backward_saved(
            normed, inv_std, slope, upstream, kernel, scale, weight_in, weight_out
        )
        grads = place(grads, input_grad, micro, micro_count)
        stored = place(stored, pre_grad, micro, micro_count)
        incoming = shifted(input_grad, "section", -1)
        return (incoming, grads, stored)

    _, grads, stores = lax.fori_loop(
        0, ticks, backward_tick, (blank, jnp.zeros(spare, jnp.bfloat16), stores)
    )
    grads = grads[1 : micro_count + 1]
    all_flat = kept[0][1 : micro_count + 1].reshape(micro_count * pixel_rows, width).astype(jnp.bfloat16)
    all_pre = stores[1 : micro_count + 1].reshape(micro_count * pixel_rows, hidden_width)
    partial = (
        lax.dot_general(
            all_pre, all_flat, (((0,), (0,)), ((), ())), preferred_element_type=jnp.float32
        )
        * factor
    )
    replicas = 1
    for name in ("z", "y", "core"):
        replicas *= lax.axis_size(name)
    share = (hidden_width // replicas) * width
    padded = -(-share // 1024) * 1024
    chunks = jnp.pad(partial.reshape(replicas, share), ((0, 0), (0, padded - share)))
    chunks = chunks.reshape(replicas, padded // 128, 128)
    for name in ("core", "y", "z"):
        bit = 1
        while bit < lax.axis_size(name):
            chunks = halve(chunks, name, bit)
            bit *= 2
    sums = chunks.reshape(padded)[:share].reshape(hidden_width // replicas, width)
    return (sums[None], grads[None])


def solution(mesh):
    sections, replicas = mesh.devices.shape
    cores = 2
    rows = int(round((replicas // cores) ** 0.5))
    split = Mesh(
        mesh.devices.reshape(sections, replicas // (rows * cores), rows, cores),
        ("section", "z", "y", "core"),
    )
    dp = ("z", "y", "core")
    return jax.shard_map(
        body,
        mesh=split,
        in_specs=(
            P(None, dp, None, None, None),
            P(None, dp, None, None, None),
            P("section", None, None),
            P("section", None),
            P("section", None, None),
            P("section", None, None),
        ),
        out_specs=(P("section", dp, None), P("section", None, dp, None, None, None)),
        check_vma=False,
    )
```

```python
import jax
import jax.numpy as jnp
from jax import lax
from jax.sharding import Mesh, PartitionSpec as P

KS = 7


EPS = 1e-06


def shifted(block, axis, distance):
    devices = range(lax.axis_size(axis))
    route = [(i - distance, i) for i in devices if i - distance in devices]
    return lax.ppermute(block, axis, route)


def depthwise(field, kernel):
    reach = KS // 2
    height = field.shape[1]
    padded = jnp.pad(field, ((0, 0), (reach, reach), (reach, reach), (0, 0)))
    total = jnp.zeros(field.shape, jnp.float32)
    for row in range(KS):
        for col in range(KS):
            total = (
                total
                + padded[:, row : row + height, col : col + height, :] * kernel[row * KS + col]
            )
    return total


def depthwise_adjoint(field, kernel):
    reach = KS // 2
    height = field.shape[1]
    padded = jnp.pad(field, ((0, 0), (reach, reach), (reach, reach), (0, 0)))
    total = jnp.zeros(field.shape, jnp.float32)
    for row in range(KS):
        for col in range(KS):
            top = 2 * reach - row
            left = 2 * reach - col
            total = (
                total
                + padded[:, top : top + height, left : left + height, :] * kernel[row * KS + col]
            )
    return total


def gelu_parts(value):
    normal_cdf = 0.5 * (1.0 + lax.erf(value * 0.7071067811865476))
    density = jnp.exp(-0.5 * value * value) * 0.3989422804014327
    return (value * normal_cdf, normal_cdf + value * density)


def block_inner(inputs, kernel, weight_in):
    width = inputs.shape[-1]
    mixed = depthwise(inputs.astype(jnp.float32), kernel)
    center = mixed - jnp.mean(mixed, axis=-1, keepdims=True)
    inv_std = lax.rsqrt(jnp.mean(center * center, axis=-1, keepdims=True) + EPS)
    normed = center * inv_std
    flat = normed.reshape(-1, width).astype(jnp.bfloat16)
    pre = lax.dot_general(
        flat, weight_in, (((1,), (1,)), ((), ())), preferred_element_type=jnp.float32
    )
    active, slope = gelu_parts(pre)
    hidden = active.astype(jnp.bfloat16)
    return (normed, inv_std, flat, slope, hidden)


def block_forward(inputs, kernel, scale, weight_in, weight_out):
    width = inputs.shape[-1]
    normed, inv_std, flat, slope, hidden = block_inner(inputs, kernel, weight_in)
    branch = jnp.dot(hidden, weight_out, preferred_element_type=jnp.float32)
    output = inputs.reshape(-1, width).astype(jnp.float32) + scale * branch
    return output.astype(jnp.bfloat16).reshape(inputs.shape)


def block_forward_saving(inputs, kernel, scale, weight_in, weight_out):
    width = inputs.shape[-1]
    normed, inv_std, flat, slope, hidden = block_inner(inputs, kernel, weight_in)
    branch = jnp.dot(hidden, weight_out, preferred_element_type=jnp.float32)
    output = inputs.reshape(-1, width).astype(jnp.float32) + scale * branch
    return (output.astype(jnp.bfloat16).reshape(inputs.shape), normed, inv_std, slope)


def block_backward_saved(normed, inv_std, slope, upstream, kernel, scale, weight_in, weight_out):
    inputs = upstream
    width = inputs.shape[-1]
    flat = normed.reshape(-1, width).astype(jnp.bfloat16)
    up_flat = upstream.reshape(-1, width).astype(jnp.float32)
    branch_grad = (scale * up_flat).astype(jnp.bfloat16)
    hidden_grad = lax.dot_general(
        branch_grad, weight_out, (((1,), (1,)), ((), ())), preferred_element_type=jnp.float32
    )
    pre_grad = (hidden_grad * slope).astype(jnp.bfloat16)
    normed_grad = jnp.dot(pre_grad, weight_in, preferred_element_type=jnp.float32).reshape(
        inputs.shape
    )
    mean_grad = jnp.mean(normed_grad, axis=-1, keepdims=True)
    mean_cross = jnp.mean(normed_grad * normed, axis=-1, keepdims=True)
    mixed_grad = inv_std * (normed_grad - mean_grad - normed * mean_cross)
    input_grad = (upstream.astype(jnp.float32) + depthwise_adjoint(mixed_grad, kernel)).astype(
        jnp.bfloat16
    )
    return (input_grad, flat, pre_grad)


def place(buffer, value, micro, count):
    slot = jnp.clip(micro, -1, count) + 1
    return lax.dynamic_update_index_in_dim(buffer, value, slot, 0)


def halve(chunks, axis, bit):
    mine = (lax.axis_index(axis) // bit) % 2
    pairs = chunks.reshape((chunks.shape[0] // 2, 2) + chunks.shape[1:])
    keep = lax.dynamic_index_in_dim(pairs, mine, 1, keepdims=False)
    send = lax.dynamic_index_in_dim(pairs, 1 - mine, 1, keepdims=False)
    route = [(i, i ^ bit) for i in range(lax.axis_size(axis))]
    arrived = lax.ppermute(send.astype(jnp.bfloat16), axis, route)
    return keep + arrived.astype(jnp.float32)


def body(images, cotangent, dw_kernel, layer_scale, w_in, w_out):
    section = lax.axis_index("section")
    sections = lax.axis_size("section")
    micro_count, img_count, side, _, width = images.shape
    kernel = lax.optimization_barrier(tuple(dw_kernel[0, tap] for tap in range(KS * KS)))
    scale = layer_scale[0]
    weight_in = w_in[0]
    weight_out = w_out[0]
    hidden_width = weight_in.shape[0]
    pixel_rows = img_count * side * side
    ticks = micro_count + sections - 1
    factor = 1.0 / (micro_count * pixel_rows)
    blank = jnp.zeros(images.shape[1:], jnp.bfloat16)

    def forward_tick(tick, carry):
        incoming, kept = carry
        micro = tick - section
        slot = jnp.clip(micro, 0, micro_count - 1)
        own = lax.dynamic_index_in_dim(images, slot, 0, keepdims=False)
        entering = jnp.where(section == 0, own, incoming)
        leaving, normed, inv_std, slope = block_forward_saving(
            entering, kernel, scale, weight_in, weight_out
        )
        kept = tuple(
            place(buffer, value, micro, micro_count)
            for buffer, value in zip(kept, (normed, inv_std, slope))
        )
        incoming = shifted(leaving, "section", 1)
        return (incoming, kept)

    spare = (micro_count + 2,) + images.shape[1:]
    kept = (
        jnp.zeros(spare, jnp.float32),
        jnp.zeros(spare[:-1] + (1,), jnp.float32),
        jnp.zeros((micro_count + 2, pixel_rows, hidden_width), jnp.float32),
    )
    _, kept = lax.fori_loop(0, ticks, forward_tick, (blank, kept))

    stores = jnp.zeros((micro_count + 2, pixel_rows, hidden_width), jnp.bfloat16)

    def backward_tick(tick, carry):
        incoming, grads, stored = carry
        micro = tick - (sections - 1 - section)
        slot = jnp.clip(micro, 0, micro_count - 1)
        own = lax.dynamic_index_in_dim(cotangent, slot, 0, keepdims=False)
        upstream = jnp.where(section == sections - 1, own, incoming)
        normed, inv_std, slope = (
            lax.dynamic_index_in_dim(buffer, slot + 1, 0, keepdims=False) for buffer in kept
        )
        input_grad, flat, pre_grad = block_backward_saved(
            normed, inv_std, slope, upstream, kernel, scale, weight_in, weight_out
        )
        grads = place(grads, input_grad, micro, micro_count)
        stored = place(stored, pre_grad, micro, micro_count)
        incoming = shifted(input_grad, "section", -1)
        return (incoming, grads, stored)

    _, grads, stores = lax.fori_loop(
        0, ticks, backward_tick, (blank, jnp.zeros(spare, jnp.bfloat16), stores)
    )
    grads = grads[1 : micro_count + 1]
    all_flat = kept[0][1 : micro_count + 1].reshape(micro_count * pixel_rows, width).astype(jnp.bfloat16)
    all_pre = stores[1 : micro_count + 1].reshape(micro_count * pixel_rows, hidden_width)
    partial = (
        lax.dot_general(
            all_pre, all_flat, (((0,), (0,)), ((), ())), preferred_element_type=jnp.float32
        )
        * factor
    )
    replicas = 1
    for name in ("z", "y", "core"):
        replicas *= lax.axis_size(name)
    share = (hidden_width // replicas) * width
    padded = -(-share // 1024) * 1024
    chunks = jnp.pad(partial.reshape(replicas, share), ((0, 0), (0, padded - share)))
    chunks = chunks.reshape(replicas, padded // 128, 128)
    for name in ("core", "y", "z"):
        bit = 1
        while bit < lax.axis_size(name):
            chunks = halve(chunks, name, bit)
            bit *= 2
    sums = chunks.reshape(padded)[:share].reshape(hidden_width // replicas, width)
    return (sums[None], grads[None])


def solution(mesh):
    sections, replicas = mesh.devices.shape
    cores = 2
    rows = int(round((replicas // cores) ** 0.5))
    split = Mesh(
        mesh.devices.reshape(sections, replicas // (rows * cores), rows, cores),
        ("section", "z", "y", "core"),
    )
    dp = ("z", "y", "core")
    return jax.shard_map(
        body,
        mesh=split,
        in_specs=(
            P(None, dp, None, None, None),
            P(None, dp, None, None, None),
            P("section", None, None),
            P("section", None),
            P("section", None, None),
            P("section", None, None),
        ),
        out_specs=(P("section", dp, None), P("section", None, dp, None, None, None)),
        check_vma=False,
    )
```

```python
import jax
import jax.numpy as jnp
from jax import lax
from jax.sharding import Mesh, PartitionSpec as P

KS = 7


EPS = 1e-06


def shifted(block, axis, distance):
    devices = range(lax.axis_size(axis))
    route = [(i - distance, i) for i in devices if i - distance in devices]
    return lax.ppermute(block, axis, route)


def depthwise(field, kernel):
    reach = KS // 2
    height = field.shape[1]
    padded = jnp.pad(field, ((0, 0), (reach, reach), (reach, reach), (0, 0)))
    total = jnp.zeros(field.shape, jnp.float32)
    for row in range(KS):
        for col in range(KS):
            total = (
                total
                + padded[:, row : row + height, col : col + height, :] * kernel[row * KS + col]
            )
    return total


def depthwise_adjoint(field, kernel):
    reach = KS // 2
    height = field.shape[1]
    padded = jnp.pad(field, ((0, 0), (reach, reach), (reach, reach), (0, 0)))
    total = jnp.zeros(field.shape, jnp.float32)
    for row in range(KS):
        for col in range(KS):
            top = 2 * reach - row
            left = 2 * reach - col
            total = (
                total
                + padded[:, top : top + height, left : left + height, :] * kernel[row * KS + col]
            )
    return total


def gelu_parts(value):
    normal_cdf = 0.5 * (1.0 + lax.erf(value * 0.7071067811865476))
    density = jnp.exp(-0.5 * value * value) * 0.3989422804014327
    return (value * normal_cdf, normal_cdf + value * density)


def block_inner(inputs, kernel, weight_in):
    width = inputs.shape[-1]
    mixed = depthwise(inputs.astype(jnp.float32), kernel)
    center = mixed - jnp.mean(mixed, axis=-1, keepdims=True)
    inv_std = lax.rsqrt(jnp.mean(center * center, axis=-1, keepdims=True) + EPS)
    normed = center * inv_std
    flat = normed.reshape(-1, width).astype(jnp.bfloat16)
    pre = lax.dot_general(
        flat, weight_in, (((1,), (1,)), ((), ())), preferred_element_type=jnp.float32
    )
    active, slope = gelu_parts(pre)
    hidden = active.astype(jnp.bfloat16)
    return (normed, inv_std, flat, slope, hidden)


def block_forward(inputs, kernel, scale, weight_in, weight_out):
    width = inputs.shape[-1]
    normed, inv_std, flat, slope, hidden = block_inner(inputs, kernel, weight_in)
    branch = jnp.dot(hidden, weight_out, preferred_element_type=jnp.float32)
    output = inputs.reshape(-1, width).astype(jnp.float32) + scale * branch
    return output.astype(jnp.bfloat16).reshape(inputs.shape)


def block_forward_saving(inputs, kernel, scale, weight_in, weight_out):
    width = inputs.shape[-1]
    normed, inv_std, flat, slope, hidden = block_inner(inputs, kernel, weight_in)
    branch = jnp.dot(hidden, weight_out, preferred_element_type=jnp.float32)
    output = inputs.reshape(-1, width).astype(jnp.float32) + scale * branch
    return (output.astype(jnp.bfloat16).reshape(inputs.shape), normed, inv_std, slope)


def block_backward_saved(normed, inv_std, slope, upstream, kernel, scale, weight_in, weight_out):
    inputs = upstream
    width = inputs.shape[-1]
    flat = normed.reshape(-1, width).astype(jnp.bfloat16)
    up_flat = upstream.reshape(-1, width).astype(jnp.float32)
    branch_grad = (scale * up_flat).astype(jnp.bfloat16)
    hidden_grad = lax.dot_general(
        branch_grad, weight_out, (((1,), (1,)), ((), ())), preferred_element_type=jnp.float32
    )
    pre_grad = (hidden_grad * slope).astype(jnp.bfloat16)
    normed_grad = jnp.dot(pre_grad, weight_in, preferred_element_type=jnp.float32).reshape(
        inputs.shape
    )
    mean_grad = jnp.mean(normed_grad, axis=-1, keepdims=True)
    mean_cross = jnp.mean(normed_grad * normed, axis=-1, keepdims=True)
    mixed_grad = inv_std * (normed_grad - mean_grad - normed * mean_cross)
    input_grad = (upstream.astype(jnp.float32) + depthwise_adjoint(mixed_grad, kernel)).astype(
        jnp.bfloat16
    )
    return (input_grad, flat, pre_grad)


def place(buffer, value, micro, count):
    slot = jnp.clip(micro, -1, count) + 1
    return lax.dynamic_update_index_in_dim(buffer, value, slot, 0)


def halve(chunks, axis, bit):
    mine = (lax.axis_index(axis) // bit) % 2
    pairs = chunks.reshape((chunks.shape[0] // 2, 2) + chunks.shape[1:])
    keep = lax.dynamic_index_in_dim(pairs, mine, 1, keepdims=False)
    send = lax.dynamic_index_in_dim(pairs, 1 - mine, 1, keepdims=False)
    route = [(i, i ^ bit) for i in range(lax.axis_size(axis))]
    arrived = lax.ppermute(send.astype(jnp.bfloat16), axis, route)
    return keep + arrived.astype(jnp.float32)


def body(images, cotangent, dw_kernel, layer_scale, w_in, w_out):
    section = lax.axis_index("section")
    sections = lax.axis_size("section")
    micro_count, img_count, side, _, width = images.shape
    kernel = lax.optimization_barrier(tuple(dw_kernel[0, tap] for tap in range(KS * KS)))
    scale = layer_scale[0]
    weight_in = w_in[0]
    weight_out = w_out[0]
    hidden_width = weight_in.shape[0]
    pixel_rows = img_count * side * side
    ticks = micro_count + sections - 1
    factor = 1.0 / (micro_count * pixel_rows)
    blank = jnp.zeros(images.shape[1:], jnp.bfloat16)

    def forward_step(tick, incoming, kept):
        micro = tick - section
        slot = jnp.clip(micro, 0, micro_count - 1)
        own = lax.dynamic_index_in_dim(images, slot, 0, keepdims=False)
        entering = jnp.where(section == 0, own, incoming)
        leaving, normed, inv_std, slope = block_forward_saving(
            entering, kernel, scale, weight_in, weight_out
        )
        kept = tuple(
            place(buffer, value, micro, micro_count)
            for buffer, value in zip(kept, (normed, inv_std, slope))
        )
        return (leaving, kept)

    def forward_tick(tick, carry):
        leaving, kept = forward_step(tick, *carry)
        return (shifted(leaving, "section", 1), kept)

    spare = (micro_count + 2,) + images.shape[1:]
    kept = (
        jnp.zeros(spare, jnp.float32),
        jnp.zeros(spare[:-1] + (1,), jnp.float32),
        jnp.zeros((micro_count + 2, pixel_rows, hidden_width), jnp.float32),
    )
    incoming, kept = lax.fori_loop(0, ticks - 1, forward_tick, (blank, kept))
    _, kept = forward_step(ticks - 1, incoming, kept)

    stores = jnp.zeros((micro_count + 2, pixel_rows, hidden_width), jnp.bfloat16)

    def backward_step(tick, incoming, grads, stored):
        micro = tick - (sections - 1 - section)
        slot = jnp.clip(micro, 0, micro_count - 1)
        own = lax.dynamic_index_in_dim(cotangent, slot, 0, keepdims=False)
        upstream = jnp.where(section == sections - 1, own, incoming)
        normed, inv_std, slope = (
            lax.dynamic_index_in_dim(buffer, slot + 1, 0, keepdims=False) for buffer in kept
        )
        input_grad, flat, pre_grad = block_backward_saved(
            normed, inv_std, slope, upstream, kernel, scale, weight_in, weight_out
        )
        grads = place(grads, input_grad, micro, micro_count)
        stored = place(stored, pre_grad, micro, micro_count)
        return (input_grad, grads, stored)

    def backward_tick(tick, carry):
        input_grad, grads, stored = backward_step(tick, *carry)
        return (shifted(input_grad, "section", -1), grads, stored)

    incoming, grads, stores = lax.fori_loop(
        0, ticks - 1, backward_tick, (blank, jnp.zeros(spare, jnp.bfloat16), stores)
    )
    _, grads, stores = backward_step(ticks - 1, incoming, grads, stores)
    grads = grads[1 : micro_count + 1]
    all_flat = kept[0][1 : micro_count + 1].reshape(micro_count * pixel_rows, width).astype(jnp.bfloat16)
    all_pre = stores[1 : micro_count + 1].reshape(micro_count * pixel_rows, hidden_width)
    partial = (
        lax.dot_general(
            all_pre, all_flat, (((0,), (0,)), ((), ())), preferred_element_type=jnp.float32
        )
        * factor
    )
    replicas = 1
    for name in ("z", "y", "core"):
        replicas *= lax.axis_size(name)
    share = (hidden_width // replicas) * width
    padded = -(-share // 1024) * 1024
    chunks = jnp.pad(partial.reshape(replicas, share), ((0, 0), (0, padded - share)))
    chunks = chunks.reshape(replicas, padded // 128, 128)
    for name in ("core", "y", "z"):
        bit = 1
        while bit < lax.axis_size(name):
            chunks = halve(chunks, name, bit)
            bit *= 2
    sums = chunks.reshape(padded)[:share].reshape(hidden_width // replicas, width)
    return (sums[None], grads[None])


def solution(mesh):
    sections, replicas = mesh.devices.shape
    cores = 2
    rows = int(round((replicas // cores) ** 0.5))
    split = Mesh(
        mesh.devices.reshape(sections, replicas // (rows * cores), rows, cores),
        ("section", "z", "y", "core"),
    )
    dp = ("z", "y", "core")
    return jax.shard_map(
        body,
        mesh=split,
        in_specs=(
            P(None, dp, None, None, None),
            P(None, dp, None, None, None),
            P("section", None, None),
            P("section", None),
            P("section", None, None),
            P("section", None, None),
        ),
        out_specs=(P("section", dp, None), P("section", None, dp, None, None, None)),
        check_vma=False,
    )
```
